256 devices in a mesh: dp: 4 (over z_hi), expert: 16 (over y, z_lo, core), mp: 4 (over x).
Axes of the slice: x: 4, y: 4, z: 8 (z_hi: 4, z_lo: 2; z = z_hi * 2 + z_lo), core: 2. Of those that a mesh axis runs over, the one named last changes fastest.
Arguments:
- hidden: bfloat16 [16384, 2048], P(('dp', 'expert', 'mp')), may hold values from -6 to 6
- norm_gain: float32 [2048], replicated, may hold values from 0.1 to 1.9
- expert_in: float32 [64, 2048, 2816], P('dp', ('expert', 'mp')), may hold values from -0.125 to 0.125
- expert_out: float32 [64, 2048, 1408], P('dp', ('expert', 'mp')), may hold values from -0.15625 to 0.15625
- expert_ids: int32 [16384, 6], P(('dp', 'expert', 'mp')), may hold values from 0 to 63, all different within a row; in each aligned block of 64 rows (0 to 63, 64 to 127, ...) at most 12 rows name the same one
- gate_levels: int32 [16384, 6], P(('dp', 'expert', 'mp')), may hold values from 1 to 255
- shared_gate: bfloat16 [2048, 2816], P(('dp', 'expert'), 'mp'), may hold values from -0.125 to 0.125
- shared_up: bfloat16 [2048, 2816], P(('dp', 'expert'), 'mp'), may hold values from -0.125 to 0.125
- shared_down: bfloat16 [2048, 2816], P(('dp', 'expert'), 'mp'), may hold values from -0.109375 to 0.109375
- next_gain: float32 [2048], replicated, may hold values from 0.1 to 1.9
- kv_weight: bfloat16 [2048, 576], P(None, 'mp'), may hold values from -0.125 to 0.125
Outputs:
- layer_out: bfloat16 [16384, 2048], P(('dp', 'expert', 'mp'))
- kv_latent: bfloat16 [16384, 576], P(('dp', 'expert'), 'mp')
The draws below stay inside these ranges and needn't reach their ends.
Inputs may be any that keep to these rules, and one draw needn't show every extreme that they name: `expert_ids`: each row names 6 different experts. Among the 64 rows of one device no expert is named by more than 12 rows, and in every draw some expert is named by exactly 12 rows of some device.
All inputs are finite; a program needn't handle non-finite values.
Results may differ from the reference program's by a relative error of at most 0.012.
Values may be sent and summed in bfloat16 or wider, within the bound.
No kernel may reach another device: no remote copies, remote signals or barrier semaphores. Data moves between devices by JAX's collectives and lax.ppermute only.
A program may use at most 128 MiB of HBM per device.

```python
import math
import jax
import jax.numpy as jnp
import numpy as np
from jax import lax

D = 2048
FF = 1408
SFF = 2816
KV = 576
TOPK = 6
TOK_DEV = 64
EXPERTS = 64
CAP = 12
TOKENS = 16384
N_MP = 4


def plant(values, key, low, largest):
    index_at = [jax.random.randint(jax.random.fold_in(key, axis), (), 0, length) for axis, length in enumerate(values.shape)]
    main_axis = values.shape.index(max(values.shape))
    beside = index_at[:main_axis] + [(index_at[main_axis] + 1) % values.shape[main_axis]] + index_at[main_axis + 1:]
    return values.at[tuple(index_at)].set(low).at[tuple(beside)].set(largest)


def block_scale(key, shape, cuts, smallest, top_value):
    level = 1.0
    for dim, blocks in cuts:
        draws = jax.random.uniform(jax.random.fold_in(jax.random.fold_in(key, 6), dim), (blocks,), jnp.float32, smallest / len(cuts), top_value / len(cuts))
        level = level * jnp.repeat(jnp.exp(draws), shape[dim] // blocks).reshape((-1,) + (1,) * (len(shape) - 1 - dim))
    return level


def routed_block(own_key, own, number, rows, number_of, top, reach, lean):
    sequence = jax.random.permutation(own_key, number_of)
    crowded, usual = load_shares(number_of, rows * top, reach, lean, True), load_shares(number_of, rows * top, reach, lean, False)
    places = jnp.arange(number_of)

    def named(lengths, rotation):
        used = int((lengths > 0).sum())
        fixed = max(1, used // 4)
        passed = fixed + (places - fixed + rotation * (used - fixed)) % max(1, number_of - fixed)
        return jnp.zeros((number_of,), jnp.int32).at[sequence[jnp.where(places < fixed, places, passed)]].set(jnp.asarray(lengths, jnp.int32))

    lengths = jnp.where(number % 4 == 0, named(crowded, number // 4), named(usual, number - number // 4 - 1))
    mixed = jax.random.permutation(jax.random.fold_in(own, 3), number_of)
    donor, taker = mixed[0:number_of // 2 * 2:2], mixed[1:number_of // 2 * 2:2]
    slack = jnp.minimum(lengths[donor] - 1, reach - lengths[taker]) // 2
    slack = jnp.where((donor == sequence[0]) | (taker == sequence[0]) | (lengths[taker] == 0), 0, jnp.maximum(slack, 0))
    passed = jax.random.randint(jax.random.fold_in(own, 4), (number_of // 2,), 0, 1 << 20) % (slack + 1)
    lengths = lengths.at[donor].add(-passed).at[taker].add(passed)
    items = jnp.searchsorted(jnp.cumsum(lengths), jnp.arange(rows * top), side="right").astype(jnp.int32)
    listing = items.reshape(top, rows).T
    listing = listing[jax.random.permutation(jax.random.fold_in(own, 1), rows)]
    rotation = jax.random.randint(jax.random.fold_in(own, 2), (rows, 1), 0, top)
    return jnp.take_along_axis(listing, (jnp.arange(top)[None, :] + rotation) % top, axis=1)


def load_shares(count, total, reach, lean, full):
    loads = [(1 << 20) // math.isqrt(grade ** lean) + 1 for grade in range(1, count + 1)]
    largest = reach if full else min(reach, max(-(-total // count), total * loads[0] // sum(loads)))
    least = 1 if total - largest >= count - 1 else 0
    given, spare = [largest] + [least] * (count - 1), total - largest - least * (count - 1)
    while spare > 0:
        candidates = [i for i in range(1, count) if given[i] < largest] or [i for i in range(1, count) if given[i] < reach]
        mass, left = sum([loads[i] for i in candidates]), spare
        for i in candidates:
            addition = min(reach - given[i], max(1, left * loads[i] // mass), spare)
            given[i] = given[i] + addition
            spare = spare - addition
    return np.array(given)


def scatter_about(rng, shape, width, limit, cuts=(), kind=jnp.bfloat16):
    entries = jax.random.normal(rng, shape, jnp.float32) * width
    if len(cuts) > 0:
        entries = block_scale(rng, shape, cuts, -0.22, 0.18) * entries
    return jnp.clip(entries, min=-limit, max=limit).astype(kind)


def setup_inputs(seed: int = 0) -> dict:
    arg_keys = jax.random.split(jax.random.key(seed), 12)
    hidden = scatter_about(arg_keys[0], (TOKENS, D), 1.0, 6.0, ((0, 256),))
    norm_gain = jnp.clip(1.0 + 0.18 * jax.random.normal(arg_keys[1], (D,), jnp.float32), 0.1, 1.9)
    expert_in = scatter_about(arg_keys[2], (EXPERTS, D, 2 * FF), D ** -0.5, 0.125, ((0, 4), (1, 64)), jnp.float32)
    expert_out = scatter_about(arg_keys[3], (EXPERTS, D, FF), FF ** -0.5, 0.15625, ((0, 4), (1, 64)), jnp.float32)
    expert_ids_keys = jax.random.split(jax.random.fold_in(arg_keys[4], 1), TOKENS // TOK_DEV)
    expert_ids_turns = jax.random.permutation(jax.random.fold_in(arg_keys[4], 3), TOKENS // TOK_DEV)
    expert_ids = jax.vmap(lambda own, number: routed_block(jax.random.fold_in(arg_keys[4], 2), own, number, TOK_DEV, EXPERTS, TOPK, CAP, 2))(expert_ids_keys, expert_ids_turns).reshape((TOKENS, TOPK))
    gate_levels = plant(jax.random.randint(arg_keys[5], (TOKENS, TOPK), 1, 256), jax.random.fold_in(arg_keys[5], 1), 1, 255).astype(jnp.int32)
    shared_gate = scatter_about(arg_keys[6], (D, SFF), D ** -0.5, 0.125, ((0, 64), (1, 4)))
    shared_up = scatter_about(arg_keys[7], (D, SFF), D ** -0.5, 0.125, ((0, 64), (1, 4)))
    shared_down = scatter_about(arg_keys[8], (D, SFF), SFF ** -0.5, 0.109375, ((0, 64), (1, 4)))
    next_gain = jnp.clip(1.0 + 0.18 * jax.random.normal(arg_keys[9], (D,), jnp.float32), 0.1, 1.9)
    kv_weight = scatter_about(arg_keys[10], (D, KV), D ** -0.5, 0.125, ((1, 4),))
    return {"hidden": hidden, "norm_gain": norm_gain, "expert_in": expert_in, "expert_out": expert_out, "expert_ids": expert_ids, "gate_levels": gate_levels, "shared_gate": shared_gate, "shared_up": shared_up, "shared_down": shared_down, "next_gain": next_gain, "kv_weight": kv_weight}


def rms_scale(values, gain):
    wide = values.astype(jnp.float32)
    mean_sq = lax.optimization_barrier(jnp.mean(wide * wide, axis=-1, keepdims=True))
    return (wide * lax.rsqrt(mean_sq + 1e-06) * gain).astype(jnp.bfloat16)

def expert_apply(rows, w_in, w_out):
    quarter = FF // N_MP
    gate_up = jnp.dot(rows, w_in, preferred_element_type=jnp.float32)
    act = (jax.nn.silu(gate_up[:, :FF]) * gate_up[:, FF:]).astype(jnp.bfloat16)
    total = jnp.zeros((rows.shape[0], rows.shape[1]), jnp.float32)
    for run in range(N_MP):
        part = lax.dot_general(act[:, run * quarter:(run + 1) * quarter], w_out[:, run * quarter:(run + 1) * quarter], (((1,), (1,)), ((), ())), preferred_element_type=jnp.float32)
        total = total + lax.optimization_barrier(part.astype(jnp.bfloat16)).astype(jnp.float32)
    return total.astype(jnp.bfloat16)

def reference(hidden, norm_gain, expert_in, expert_out, expert_ids, gate_levels, shared_gate, shared_up, shared_down, next_gain, kv_weight):
    normed = rms_scale(hidden, norm_gain)
    levels = gate_levels.astype(jnp.float32)
    gate_weights = levels / lax.optimization_barrier(jnp.sum(levels, axis=1, keepdims=True))
    pair_ids = expert_ids.reshape(-1)
    pair_token = (jnp.arange(TOKENS * TOPK, dtype=jnp.int32) // TOPK).astype(jnp.int32)
    buffer_rows = CAP * (TOKENS // TOK_DEV)

    def one_expert(routed, inputs):
        index, w_in, w_out = inputs
        member = pair_ids == index
        position = (jnp.cumsum(member.astype(jnp.int32)) - 1).astype(jnp.int32)
        target = jnp.where(member, position, buffer_rows).astype(jnp.int32)
        token_of_slot = jnp.zeros((buffer_rows,), jnp.int32).at[target].set(pair_token, mode='drop')
        rows = normed[token_of_slot]
        result = expert_apply(rows, w_in.astype(jnp.bfloat16), w_out.astype(jnp.bfloat16))
        member_pairs = member.reshape(TOKENS, TOPK)
        pos_pairs = jnp.where(member, position, 0).astype(jnp.int32).reshape(TOKENS, TOPK)
        for slot_k in range(TOPK):
            weight = jnp.where(member_pairs[:, slot_k], gate_weights[:, slot_k], 0.0)
            routed = routed + weight[:, None] * result[pos_pairs[:, slot_k]].astype(jnp.float32)
        return (routed, None)
    routed, _ = lax.scan(one_expert, jnp.zeros((TOKENS, D), jnp.float32), (jnp.arange(EXPERTS, dtype=jnp.int32), expert_in, expert_out))
    gate_part = jnp.dot(normed, shared_gate, preferred_element_type=jnp.float32)
    up_part = jnp.dot(normed, shared_up, preferred_element_type=jnp.float32)
    shared_act = (jax.nn.silu(gate_part) * up_part).astype(jnp.bfloat16)
    shared_out = lax.dot_general(shared_act, shared_down, (((1,), (1,)), ((), ())), preferred_element_type=jnp.float32)
    layer_out = (hidden.astype(jnp.float32) + routed + shared_out).astype(jnp.bfloat16)
    next_normed = rms_scale(layer_out, next_gain)
    kv_latent = jnp.dot(next_normed, kv_weight, preferred_element_type=jnp.float32).astype(jnp.bfloat16)
    return (layer_out, kv_latent)
```

```python
import jax
import jax.numpy as jnp
from jax import lax
from jax.sharding import PartitionSpec as P


def rms_scale(values, gain):
    wide = values.astype(jnp.float32)
    mean_sq = jnp.mean(wide * wide, axis=-1, keepdims=True)
    return (wide * lax.rsqrt(mean_sq + 1e-06) * gain).astype(jnp.bfloat16)


def expert_part(rows, gate_up_w, down_w):
    quarter = down_w.shape[1]
    gate_up = jnp.dot(rows, gate_up_w, preferred_element_type=jnp.float32)
    act = (jax.nn.silu(gate_up[:, :quarter]) * gate_up[:, quarter:]).astype(jnp.bfloat16)
    return lax.dot_general(
        act, down_w, (((1,), (1,)), ((), ())), preferred_element_type=jnp.float32
    )


def on_device(
    hidden,
    norm_gain,
    expert_in,
    expert_out,
    expert_ids,
    gate_levels,
    shared_gate,
    shared_up,
    shared_down,
    next_gain,
    kv_weight,
):
    tok_rows, width = hidden.shape
    top = expert_ids.shape[1]
    n_mp = lax.axis_size("mp")
    n_groups = lax.axis_size(("dp", "expert"))
    capacity = min(tok_rows, (2 * tok_rows * top + n_groups - 1) // n_groups)
    local_e, local_rows, double = expert_in.shape
    full_ff = double // 2
    quarter = full_ff // n_mp
    in_cast = (
        expert_in.astype(jnp.bfloat16)
        .reshape(local_e, local_rows, 2, n_mp, quarter)
        .transpose(0, 3, 1, 2, 4)
    )
    out_cast = (
        expert_out.astype(jnp.bfloat16)
        .reshape(local_e, local_rows, n_mp, quarter)
        .transpose(0, 2, 1, 3)
    )
    in_send = in_cast.reshape(local_e * n_mp, local_rows, 2, quarter)
    out_send = out_cast.reshape(local_e * n_mp, local_rows, quarter)
    in_recv, out_recv = (
        lax.all_to_all(in_send, ("expert", "mp"), split_axis=0, concat_axis=1, tiled=True),
        lax.all_to_all(out_send, ("expert", "mp"), split_axis=0, concat_axis=1, tiled=True),
    )
    gate_up_w = in_recv.reshape(width, 2 * quarter)
    down_w = out_recv.reshape(width, quarter)
    normed = rms_scale(hidden, norm_gain)
    levels = gate_levels.astype(jnp.float32)
    gate_weights = levels / jnp.sum(levels, axis=1, keepdims=True)
    flat_ids = expert_ids.reshape(-1)
    pairs = flat_ids.shape[0]
    onehot = (flat_ids[:, None] == jnp.arange(n_groups, dtype=jnp.int32)[None, :]).astype(jnp.int32)
    before = jnp.cumsum(onehot, axis=0) - onehot
    slot_of_pair = jnp.sum(before * onehot, axis=1)
    target = flat_ids * capacity + slot_of_pair
    token_of_pair = jnp.arange(pairs, dtype=jnp.int32) // top
    send = (
        jnp.zeros((n_groups * capacity, width), jnp.bfloat16).at[target].set(normed[token_of_pair])
    )
    received = lax.all_to_all(
        send.reshape(n_groups, capacity, width),
        ("dp", "expert"),
        split_axis=0,
        concat_axis=0,
        tiled=True,
    )
    slots_here = received.reshape(n_groups * capacity, width)
    every_slot = lax.all_gather(slots_here, "mp", axis=0, tiled=True)
    rows = every_slot
    summed = lax.psum_scatter(
        expert_part(rows, gate_up_w, down_w).astype(jnp.bfloat16),
        "mp",
        scatter_dimension=0,
        tiled=True,
    )
    result = summed.reshape(n_groups, capacity, width)
    back = lax.all_to_all(
        result, ("dp", "expert"), split_axis=0, concat_axis=0, tiled=True
    ).reshape(n_groups * capacity, width)
    picked = back[target].reshape(tok_rows, top, width)
    routed = jnp.sum(picked.astype(jnp.float32) * gate_weights[:, :, None], axis=1)
    shared_cols = shared_gate.shape[1]
    shared_cat = jnp.concatenate([shared_gate, shared_up, shared_down], axis=1)
    shared_cat = lax.all_gather(shared_cat, "dp", axis=0, tiled=False)
    shared_cat = lax.all_gather(shared_cat, "expert", axis=1, tiled=False)
    shared_cat = shared_cat.reshape(width, 3 * shared_cols)
    gate_w = shared_cat[:, :shared_cols]
    up_w = shared_cat[:, shared_cols : 2 * shared_cols]
    down_s = shared_cat[:, 2 * shared_cols :]
    group_rows = lax.all_gather(normed, "mp", axis=0, tiled=True)
    rows = group_rows
    gate_part = jnp.dot(rows, gate_w, preferred_element_type=jnp.float32)
    up_part = jnp.dot(rows, up_w, preferred_element_type=jnp.float32)
    act = (jax.nn.silu(gate_part) * up_part).astype(jnp.bfloat16)
    shared_out = lax.psum_scatter(
        lax.dot_general(act, down_s, (((1,), (1,)), ((), ())), preferred_element_type=jnp.float32),
        "mp",
        scatter_dimension=0,
        tiled=True,
    )
    layer_out = (hidden.astype(jnp.float32) + routed + shared_out).astype(jnp.bfloat16)
    next_rows = rms_scale(layer_out, next_gain)
    next_group = lax.all_gather(next_rows, "mp", axis=0, tiled=True)
    kv_latent = jnp.dot(next_group, kv_weight, preferred_element_type=jnp.float32).astype(
        jnp.bfloat16
    )
    return (layer_out, kv_latent)


def solution(mesh):
    in_specs = (
        P(("dp", "expert", "mp"), None),
        P(),
        P("dp", ("expert", "mp"), None),
        P("dp", ("expert", "mp"), None),
        P(("dp", "expert", "mp"), None),
        P(("dp", "expert", "mp"), None),
        P(("dp", "expert"), "mp"),
        P(("dp", "expert"), "mp"),
        P(("dp", "expert"), "mp"),
        P(),
        P(None, "mp"),
    )
    out_specs = (P(("dp", "expert", "mp"), None), P(("dp", "expert"), "mp"))
    return jax.shard_map(
        on_device, mesh=mesh, in_specs=in_specs, out_specs=out_specs, check_vma=False
    )
```

```python
import jax
import jax.numpy as jnp
from jax import lax
from jax.sharding import PartitionSpec as P


def rms_scale(values, gain):
    wide = values.astype(jnp.float32)
    mean_sq = jnp.mean(wide * wide, axis=-1, keepdims=True)
    return (wide * lax.rsqrt(mean_sq + 1e-06) * gain).astype(jnp.bfloat16)


def expert_part(rows, gate_up_w, down_w):
    quarter = down_w.shape[1]
    gate_up = jnp.dot(rows, gate_up_w, preferred_element_type=jnp.float32)
    act = (jax.nn.silu(gate_up[:, :quarter]) * gate_up[:, quarter:]).astype(jnp.bfloat16)
    return lax.dot_general(
        act, down_w, (((1,), (1,)), ((), ())), preferred_element_type=jnp.float32
    )


def on_device(
    hidden,
    norm_gain,
    expert_in,
    expert_out,
    expert_ids,
    gate_levels,
    shared_gate,
    shared_up,
    shared_down,
    next_gain,
    kv_weight,
):
    tok_rows, width = hidden.shape
    top = expert_ids.shape[1]
    n_mp = lax.axis_size("mp")
    n_groups = lax.axis_size(("dp", "expert"))
    capacity = min(tok_rows, (2 * tok_rows * top + n_groups - 1) // n_groups)
    local_e, local_rows, double = expert_in.shape
    full_ff = double // 2
    quarter = full_ff // n_mp
    in_cast = (
        expert_in.astype(jnp.bfloat16)
        .reshape(local_e, local_rows, 2, n_mp, quarter)
        .transpose(0, 3, 1, 2, 4)
    )
    out_cast = (
        expert_out.astype(jnp.bfloat16)
        .reshape(local_e, local_rows, n_mp, quarter)
        .transpose(0, 2, 1, 3)
    )
    in_send = in_cast.reshape(local_e * n_mp, local_rows, 2, quarter)
    out_send = out_cast.reshape(local_e * n_mp, local_rows, quarter)
    in_recv, out_recv = (
        lax.all_to_all(in_send, ("expert", "mp"), split_axis=0, concat_axis=1, tiled=True),
        lax.all_to_all(out_send, ("expert", "mp"), split_axis=0, concat_axis=1, tiled=True),
    )
    gate_up_w = in_recv.reshape(width, 2 * quarter)
    down_w = out_recv.reshape(width, quarter)
    normed = rms_scale(hidden, norm_gain)
    levels = gate_levels.astype(jnp.float32)
    gate_weights = levels / jnp.sum(levels, axis=1, keepdims=True)
    flat_ids = expert_ids.reshape(-1)
    pairs = flat_ids.shape[0]
    onehot = (flat_ids[:, None] == jnp.arange(n_groups, dtype=jnp.int32)[None, :]).astype(jnp.int32)
    before = jnp.cumsum(onehot, axis=0) - onehot
    slot_of_pair = jnp.sum(before * onehot, axis=1)
    target = flat_ids * capacity + slot_of_pair
    token_of_pair = jnp.arange(pairs, dtype=jnp.int32) // top
    send = (
        jnp.zeros((n_groups * capacity, width), jnp.bfloat16).at[target].set(normed[token_of_pair])
    )
    received = lax.all_to_all(
        send.reshape(n_groups, capacity, width),
        ("dp", "expert"),
        split_axis=0,
        concat_axis=0,
        tiled=True,
    )
    shared_cols = shared_gate.shape[1]
    shared_cat = jnp.concatenate([shared_gate, shared_up, shared_down], axis=1)
    shared_cat = lax.all_gather(shared_cat, "dp", axis=0, tiled=False)
    shared_cat = lax.all_gather(shared_cat, "expert", axis=1, tiled=False)
    shared_cat = shared_cat.reshape(width, 3 * shared_cols)
    group_rows = lax.all_gather(normed, "mp", axis=0, tiled=True)
    received, shared_cat, group_rows = lax.optimization_barrier(
        (received, shared_cat, group_rows)
    )
    slots_here = received.reshape(n_groups * capacity, width)
    every_slot = lax.all_gather(slots_here, "mp", axis=0, tiled=True)
    rows = every_slot
    summed = lax.psum_scatter(
        expert_part(rows, gate_up_w, down_w).astype(jnp.bfloat16),
        "mp",
        scatter_dimension=0,
        tiled=True,
    )
    result = summed.reshape(n_groups, capacity, width)
    back = lax.all_to_all(
        result, ("dp", "expert"), split_axis=0, concat_axis=0, tiled=True
    ).reshape(n_groups * capacity, width)
    picked = back[target].reshape(tok_rows, top, width)
    routed = jnp.sum(picked.astype(jnp.float32) * gate_weights[:, :, None], axis=1)
    gate_w = shared_cat[:, :shared_cols]
    up_w = shared_cat[:, shared_cols : 2 * shared_cols]
    down_s = shared_cat[:, 2 * shared_cols :]
    rows = group_rows
    gate_part = jnp.dot(rows, gate_w, preferred_element_type=jnp.float32)
    up_part = jnp.dot(rows, up_w, preferred_element_type=jnp.float32)
    act = (jax.nn.silu(gate_part) * up_part).astype(jnp.bfloat16)
    shared_out = lax.psum_scatter(
        lax.dot_general(act, down_s, (((1,), (1,)), ((), ())), preferred_element_type=jnp.float32),
        "mp",
        scatter_dimension=0,
        tiled=True,
    )
    layer_out = (hidden.astype(jnp.float32) + routed + shared_out).astype(jnp.bfloat16)
    next_rows = rms_scale(layer_out, next_gain)
    next_group = lax.all_gather(next_rows, "mp", axis=0, tiled=True)
    kv_latent = jnp.dot(next_group, kv_weight, preferred_element_type=jnp.float32).astype(
        jnp.bfloat16
    )
    return (layer_out, kv_latent)


def solution(mesh):
    in_specs = (
        P(("dp", "expert", "mp"), None),
        P(),
        P("dp", ("expert", "mp"), None),
        P("dp", ("expert", "mp"), None),
        P(("dp", "expert", "mp"), None),
        P(("dp", "expert", "mp"), None),
        P(("dp", "expert"), "mp"),
        P(("dp", "expert"), "mp"),
        P(("dp", "expert"), "mp"),
        P(),
        P(None, "mp"),
    )
    out_specs = (P(("dp", "expert", "mp"), None), P(("dp", "expert"), "mp"))
    return jax.shard_map(
        on_device, mesh=mesh, in_specs=in_specs, out_specs=out_specs, check_vma=False
    )
```

```python
import jax
import jax.numpy as jnp
from jax import lax
from jax.sharding import PartitionSpec as P


def rms_scale(values, gain):
    wide = values.astype(jnp.float32)
    mean_sq = jnp.mean(wide * wide, axis=-1, keepdims=True)
    return (wide * lax.rsqrt(mean_sq + 1e-06) * gain).astype(jnp.bfloat16)


def expert_part(rows, gate_up_w, down_w):
    quarter = down_w.shape[1]
    gate_up = jnp.dot(rows, gate_up_w, preferred_element_type=jnp.float32)
    act = (jax.nn.silu(gate_up[:, :quarter]) * gate_up[:, quarter:]).astype(jnp.bfloat16)
    return lax.dot_general(
        act, down_w, (((1,), (1,)), ((), ())), preferred_element_type=jnp.float32
    )


def on_device(
    hidden,
    norm_gain,
    expert_in,
    expert_out,
    expert_ids,
    gate_levels,
    shared_gate,
    shared_up,
    shared_down,
    next_gain,
    kv_weight,
):
    tok_rows, width = hidden.shape
    top = expert_ids.shape[1]
    n_mp = lax.axis_size("mp")
    n_groups = lax.axis_size(("dp", "expert"))
    capacity = min(tok_rows, (2 * tok_rows * top + n_groups - 1) // n_groups)
    local_e, local_rows, double = expert_in.shape
    full_ff = double // 2
    quarter = full_ff // n_mp
    in_cast = (
        expert_in.astype(jnp.bfloat16)
        .reshape(local_e, local_rows, 2, n_mp, quarter)
        .transpose(0, 3, 1, 2, 4)
    )
    out_cast = (
        expert_out.astype(jnp.bfloat16)
        .reshape(local_e, local_rows, n_mp, quarter)
        .transpose(0, 2, 1, 3)
    )
    in_send = in_cast.reshape(local_e * n_mp, local_rows, 2, quarter)
    out_send = out_cast.reshape(local_e * n_mp, local_rows, quarter)
    in_recv, out_recv = (
        lax.all_to_all(in_send, ("expert", "mp"), split_axis=0, concat_axis=1, tiled=True),
        lax.all_to_all(out_send, ("expert", "mp"), split_axis=0, concat_axis=1, tiled=True),
    )
    gate_up_w = in_recv.reshape(width, 2 * quarter)
    down_w = out_recv.reshape(width, quarter)
    normed = rms_scale(hidden, norm_gain)
    levels = gate_levels.astype(jnp.float32)
    gate_weights = levels / jnp.sum(levels, axis=1, keepdims=True)
    flat_ids = expert_ids.reshape(-1)
    pairs = flat_ids.shape[0]
    onehot = (flat_ids[:, None] == jnp.arange(n_groups, dtype=jnp.int32)[None, :]).astype(jnp.int32)
    before = jnp.cumsum(onehot, axis=0) - onehot
    slot_of_pair = jnp.sum(before * onehot, axis=1)
    target = flat_ids * capacity + slot_of_pair
    token_of_pair = jnp.arange(pairs, dtype=jnp.int32) // top
    send = (
        jnp.zeros((n_groups * capacity, width), jnp.bfloat16).at[target].set(normed[token_of_pair])
    )
    n_chunks = 2 if capacity % 2 == 0 else 1
    chunk = capacity // n_chunks
    send = send.reshape(n_groups, capacity, width)
    received = [
        lax.all_to_all(
            send[:, c * chunk : (c + 1) * chunk],
            ("dp", "expert"),
            split_axis=0,
            concat_axis=0,
            tiled=True,
        )
        for c in range(n_chunks)
    ]
    shared_cols = shared_gate.shape[1]
    shared_cat = jnp.concatenate([shared_gate, shared_up, shared_down], axis=1)
    shared_cat = lax.all_gather(shared_cat, "dp", axis=0, tiled=False)
    shared_cat = lax.all_gather(shared_cat, "expert", axis=1, tiled=False)
    shared_cat = shared_cat.reshape(width, 3 * shared_cols)
    group_rows = lax.all_gather(normed, "mp", axis=0, tiled=True)
    received[0], shared_cat, group_rows = lax.optimization_barrier(
        (received[0], shared_cat, group_rows)
    )
    back = []
    for c in range(n_chunks):
        slots_here = received[c].reshape(n_groups * chunk, width)
        rows = lax.all_gather(slots_here, "mp", axis=0, tiled=True)
        summed = lax.psum_scatter(
            expert_part(rows, gate_up_w, down_w).astype(jnp.bfloat16),
            "mp",
            scatter_dimension=0,
            tiled=True,
        )
        back.append(
            lax.all_to_all(
                summed.reshape(n_groups, chunk, width),
                ("dp", "expert"),
                split_axis=0,
                concat_axis=0,
                tiled=True,
            )
        )
    back = jnp.concatenate(back, axis=1).reshape(n_groups * capacity, width)
    picked = back[target].reshape(tok_rows, top, width)
    routed = jnp.sum(picked.astype(jnp.float32) * gate_weights[:, :, None], axis=1)
    gate_w = shared_cat[:, :shared_cols]
    up_w = shared_cat[:, shared_cols : 2 * shared_cols]
    down_s = shared_cat[:, 2 * shared_cols :]
    rows = group_rows
    gate_part = jnp.dot(rows, gate_w, preferred_element_type=jnp.float32)
    up_part = jnp.dot(rows, up_w, preferred_element_type=jnp.float32)
    act = (jax.nn.silu(gate_part) * up_part).astype(jnp.bfloat16)
    shared_out = lax.psum_scatter(
        lax.dot_general(act, down_s, (((1,), (1,)), ((), ())), preferred_element_type=jnp.float32),
        "mp",
        scatter_dimension=0,
        tiled=True,
    )
    layer_out = (hidden.astype(jnp.float32) + routed + shared_out).astype(jnp.bfloat16)
    next_rows = rms_scale(layer_out, next_gain)
    next_group = lax.all_gather(next_rows, "mp", axis=0, tiled=True)
    kv_latent = jnp.dot(next_group, kv_weight, preferred_element_type=jnp.float32).astype(
        jnp.bfloat16
    )
    return (layer_out, kv_latent)


def solution(mesh):
    in_specs = (
        P(("dp", "expert", "mp"), None),
        P(),
        P("dp", ("expert", "mp"), None),
        P("dp", ("expert", "mp"), None),
        P(("dp", "expert", "mp"), None),
        P(("dp", "expert", "mp"), None),
        P(("dp", "expert"), "mp"),
        P(("dp", "expert"), "mp"),
        P(("dp", "expert"), "mp"),
        P(),
        P(None, "mp"),
    )
    out_specs = (P(("dp", "expert", "mp"), None), P(("dp", "expert"), "mp"))
    return jax.shard_map(
        on_device, mesh=mesh, in_specs=in_specs, out_specs=out_specs, check_vma=False
    )
```

```python
import jax
import jax.numpy as jnp
from jax import lax
from jax.sharding import PartitionSpec as P


def rms_scale(values, gain):
    wide = values.astype(jnp.float32)
    mean_sq = jnp.mean(wide * wide, axis=-1, keepdims=True)
    return (wide * lax.rsqrt(mean_sq + 1e-06) * gain).astype(jnp.bfloat16)


def expert_part(rows, gate_up_w, down_w):
    quarter = down_w.shape[1]
    gate_up = jnp.dot(rows, gate_up_w, preferred_element_type=jnp.float32)
    act = (jax.nn.silu(gate_up[:, :quarter]) * gate_up[:, quarter:]).astype(jnp.bfloat16)
    return lax.dot_general(
        act, down_w, (((1,), (1,)), ((), ())), preferred_element_type=jnp.float32
    )


def on_device(
    hidden,
    norm_gain,
    expert_in,
    expert_out,
    expert_ids,
    gate_levels,
    shared_gate,
    shared_up,
    shared_down,
    next_gain,
    kv_weight,
):
    tok_rows, width = hidden.shape
    top = expert_ids.shape[1]
    n_mp = lax.axis_size("mp")
    n_groups = lax.axis_size(("dp", "expert"))
    capacity = min(tok_rows, (2 * tok_rows * top + n_groups - 1) // n_groups)
    local_e, local_rows, double = expert_in.shape
    full_ff = double // 2
    quarter = full_ff // n_mp
    in_cast = (
        expert_in.astype(jnp.bfloat16)
        .reshape(local_e, local_rows, 2, n_mp, quarter)
        .transpose(0, 3, 1, 2, 4)
    )
    out_cast = (
        expert_out.astype(jnp.bfloat16)
        .reshape(local_e, local_rows, n_mp, quarter)
        .transpose(0, 2, 1, 3)
    )
    in_send = in_cast.reshape(local_e * n_mp, local_rows, 2, quarter)
    out_send = out_cast.reshape(local_e * n_mp, local_rows, quarter)
    in_recv, out_recv = (
        lax.all_to_all(in_send, ("expert", "mp"), split_axis=0, concat_axis=1, tiled=True),
        lax.all_to_all(out_send, ("expert", "mp"), split_axis=0, concat_axis=1, tiled=True),
    )
    gate_up_w = in_recv.reshape(width, 2 * quarter)
    down_w = out_recv.reshape(width, quarter)
    normed = rms_scale(hidden, norm_gain)
    levels = gate_levels.astype(jnp.float32)
    gate_weights = levels / jnp.sum(levels, axis=1, keepdims=True)
    flat_ids = expert_ids.reshape(-1)
    pairs = flat_ids.shape[0]
    onehot = (flat_ids[:, None] == jnp.arange(n_groups, dtype=jnp.int32)[None, :]).astype(jnp.int32)
    before = jnp.cumsum(onehot, axis=0) - onehot
    slot_of_pair = jnp.sum(before * onehot, axis=1)
    target = flat_ids * capacity + slot_of_pair
    token_of_pair = jnp.arange(pairs, dtype=jnp.int32) // top
    slot_ids = jnp.arange(n_groups * capacity, dtype=jnp.int32)
    token_slot = target.reshape(tok_rows, top)[:, :, None] == slot_ids[None, None, :]
    slot_token = jnp.any(token_slot, axis=1).astype(jnp.bfloat16)
    send = lax.dot_general(
        slot_token, normed, (((0,), (0,)), ((), ())), preferred_element_type=jnp.float32
    ).astype(jnp.bfloat16)
    n_chunks = 2 if capacity % 2 == 0 else 1
    chunk = capacity // n_chunks
    send = send.reshape(n_groups, capacity, width)
    received = [
        lax.all_to_all(
            send[:, c * chunk : (c + 1) * chunk],
            ("dp", "expert"),
            split_axis=0,
            concat_axis=0,
            tiled=True,
        )
        for c in range(n_chunks)
    ]
    shared_cols = shared_gate.shape[1]
    shared_cat = jnp.concatenate([shared_gate, shared_up, shared_down], axis=1)
    shared_cat = lax.all_gather(shared_cat, "dp", axis=0, tiled=False)
    shared_cat = lax.all_gather(shared_cat, "expert", axis=1, tiled=False)
    shared_cat = shared_cat.reshape(width, 3 * shared_cols)
    group_rows = lax.all_gather(normed, "mp", axis=0, tiled=True)
    received[0], shared_cat, group_rows = lax.optimization_barrier(
        (received[0], shared_cat, group_rows)
    )
    back = []
    for c in range(n_chunks):
        slots_here = received[c].reshape(n_groups * chunk, width)
        rows = lax.all_gather(slots_here, "mp", axis=0, tiled=True)
        summed = lax.psum_scatter(
            expert_part(rows, gate_up_w, down_w).astype(jnp.bfloat16),
            "mp",
            scatter_dimension=0,
            tiled=True,
        )
        back.append(
            lax.all_to_all(
                summed.reshape(n_groups, chunk, width),
                ("dp", "expert"),
                split_axis=0,
                concat_axis=0,
                tiled=True,
            )
        )
    back = jnp.concatenate(back, axis=1).reshape(n_groups * capacity, width)
    slot_weight = jnp.sum(jnp.where(token_slot, gate_weights[:, :, None], 0.0), axis=1)
    routed = jnp.dot(
        slot_weight,
        back.astype(jnp.float32),
        precision=lax.Precision.HIGHEST,
        preferred_element_type=jnp.float32,
    )
    gate_w = shared_cat[:, :shared_cols]
    up_w = shared_cat[:, shared_cols : 2 * shared_cols]
    down_s = shared_cat[:, 2 * shared_cols :]
    rows = group_rows
    gate_part = jnp.dot(rows, gate_w, preferred_element_type=jnp.float32)
    up_part = jnp.dot(rows, up_w, preferred_element_type=jnp.float32)
    act = (jax.nn.silu(gate_part) * up_part).astype(jnp.bfloat16)
    shared_out = lax.psum_scatter(
        lax.dot_general(act, down_s, (((1,), (1,)), ((), ())), preferred_element_type=jnp.float32),
        "mp",
        scatter_dimension=0,
        tiled=True,
    )
    layer_out = (hidden.astype(jnp.float32) + routed + shared_out).astype(jnp.bfloat16)
    next_rows = rms_scale(layer_out, next_gain)
    next_group = lax.all_gather(next_rows, "mp", axis=0, tiled=True)
    kv_latent = jnp.dot(next_group, kv_weight, preferred_element_type=jnp.float32).astype(
        jnp.bfloat16
    )
    return (layer_out, kv_latent)


def solution(mesh):
    in_specs = (
        P(("dp", "expert", "mp"), None),
        P(),
        P("dp", ("expert", "mp"), None),
        P("dp", ("expert", "mp"), None),
        P(("dp", "expert", "mp"), None),
        P(("dp", "expert", "mp"), None),
        P(("dp", "expert"), "mp"),
        P(("dp", "expert"), "mp"),
        P(("dp", "expert"), "mp"),
        P(),
        P(None, "mp"),
    )
    out_specs = (P(("dp", "expert", "mp"), None), P(("dp", "expert"), "mp"))
    return jax.shard_map(
        on_device, mesh=mesh, in_specs=in_specs, out_specs=out_specs, check_vma=False
    )
```

```python
import jax
import jax.numpy as jnp
from jax import lax
from jax.sharding import PartitionSpec as P


def rms_scale(values, gain):
    wide = values.astype(jnp.float32)
    mean_sq = jnp.mean(wide * wide, axis=-1, keepdims=True)
    return (wide * lax.rsqrt(mean_sq + 1e-06) * gain).astype(jnp.bfloat16)


def expert_part(rows, gate_up_w, down_w):
    quarter = down_w.shape[1]
    gate_up = jnp.dot(rows, gate_up_w, preferred_element_type=jnp.float32)
    act = (jax.nn.silu(gate_up[:, :quarter]) * gate_up[:, quarter:]).astype(jnp.bfloat16)
    return lax.dot_general(
        act, down_w, (((1,), (1,)), ((), ())), preferred_element_type=jnp.float32
    )


def on_device(
    hidden,
    norm_gain,
    expert_in,
    expert_out,
    expert_ids,
    gate_levels,
    shared_gate,
    shared_up,
    shared_down,
    next_gain,
    kv_weight,
):
    tok_rows, width = hidden.shape
    top = expert_ids.shape[1]
    n_mp = lax.axis_size("mp")
    n_groups = lax.axis_size(("dp", "expert"))
    capacity = min(tok_rows, (2 * tok_rows * top + n_groups - 1) // n_groups)
    local_e, local_rows, double = expert_in.shape
    full_ff = double // 2
    quarter = full_ff // n_mp
    in_cast = (
        expert_in.astype(jnp.bfloat16)
        .reshape(local_e, local_rows, 2, n_mp, quarter)
        .transpose(0, 3, 1, 2, 4)
    )
    out_cast = (
        expert_out.astype(jnp.bfloat16)
        .reshape(local_e, local_rows, n_mp, quarter)
        .transpose(0, 2, 1, 3)
    )
    in_send = in_cast.reshape(local_e * n_mp, local_rows, 2, quarter)
    out_send = out_cast.reshape(local_e * n_mp, local_rows, quarter)
    in_recv, out_recv = (
        lax.all_to_all(in_send, ("expert", "mp"), split_axis=0, concat_axis=1, tiled=True),
        lax.all_to_all(out_send, ("expert", "mp"), split_axis=0, concat_axis=1, tiled=True),
    )
    gate_up_w = in_recv.reshape(width, 2 * quarter)
    down_w = out_recv.reshape(width, quarter)
    normed = rms_scale(hidden, norm_gain)
    levels = gate_levels.astype(jnp.float32)
    gate_weights = levels / jnp.sum(levels, axis=1, keepdims=True)
    flat_ids = expert_ids.reshape(-1)
    pairs = flat_ids.shape[0]
    onehot = (flat_ids[:, None] == jnp.arange(n_groups, dtype=jnp.int32)[None, :]).astype(jnp.int32)
    before = jnp.cumsum(onehot, axis=0) - onehot
    slot_of_pair = jnp.sum(before * onehot, axis=1)
    target = flat_ids * capacity + slot_of_pair
    token_of_pair = jnp.arange(pairs, dtype=jnp.int32) // top
    slot_ids = jnp.arange(n_groups * capacity, dtype=jnp.int32)
    token_slot = target.reshape(tok_rows, top)[:, :, None] == slot_ids[None, None, :]
    slot_token = jnp.any(token_slot, axis=1).astype(jnp.bfloat16)
    send = lax.dot_general(
        slot_token, normed, (((0,), (0,)), ((), ())), preferred_element_type=jnp.float32
    ).astype(jnp.bfloat16)
    n_chunks = 3 if capacity % 3 == 0 else 1
    chunk = capacity // n_chunks
    send = send.reshape(n_groups, capacity, width)
    received = [
        lax.all_to_all(
            send[:, c * chunk : (c + 1) * chunk],
            ("dp", "expert"),
            split_axis=0,
            concat_axis=0,
            tiled=True,
        )
        for c in range(n_chunks)
    ]
    shared_cols = shared_gate.shape[1]
    shared_cat = jnp.concatenate([shared_gate, shared_up, shared_down], axis=1)
    shared_cat = lax.all_gather(shared_cat, "dp", axis=0, tiled=False)
    shared_cat = lax.all_gather(shared_cat, "expert", axis=1, tiled=False)
    shared_cat = shared_cat.reshape(width, 3 * shared_cols)
    group_rows = lax.all_gather(normed, "mp", axis=0, tiled=True)
    received[0], shared_cat, group_rows = lax.optimization_barrier(
        (received[0], shared_cat, group_rows)
    )
    back = []
    for c in range(n_chunks):
        slots_here = received[c].reshape(n_groups * chunk, width)
        rows = lax.all_gather(slots_here, "mp", axis=0, tiled=True)
        summed = lax.psum_scatter(
            expert_part(rows, gate_up_w, down_w).astype(jnp.bfloat16),
            "mp",
            scatter_dimension=0,
            tiled=True,
        )
        back.append(
            lax.all_to_all(
                summed.reshape(n_groups, chunk, width),
                ("dp", "expert"),
                split_axis=0,
                concat_axis=0,
                tiled=True,
            )
        )
    back = jnp.concatenate(back, axis=1).reshape(n_groups * capacity, width)
    slot_weight = jnp.sum(jnp.where(token_slot, gate_weights[:, :, None], 0.0), axis=1)
    routed = jnp.dot(
        slot_weight,
        back.astype(jnp.float32),
        precision=lax.Precision.HIGHEST,
        preferred_element_type=jnp.float32,
    )
    gate_w = shared_cat[:, :shared_cols]
    up_w = shared_cat[:, shared_cols : 2 * shared_cols]
    down_s = shared_cat[:, 2 * shared_cols :]
    rows = group_rows
    gate_part = jnp.dot(rows, gate_w, preferred_element_type=jnp.float32)
    up_part = jnp.dot(rows, up_w, preferred_element_type=jnp.float32)
    act = (jax.nn.silu(gate_part) * up_part).astype(jnp.bfloat16)
    shared_out = lax.psum_scatter(
        lax.dot_general(act, down_s, (((1,), (1,)), ((), ())), preferred_element_type=jnp.float32),
        "mp",
        scatter_dimension=0,
        tiled=True,
    )
    layer_out = (hidden.astype(jnp.float32) + routed + shared_out).astype(jnp.bfloat16)
    next_rows = rms_scale(layer_out, next_gain)
    next_group = lax.all_gather(next_rows, "mp", axis=0, tiled=True)
    kv_latent = jnp.dot(next_group, kv_weight, preferred_element_type=jnp.float32).astype(
        jnp.bfloat16
    )
    return (layer_out, kv_latent)


def solution(mesh):
    in_specs = (
        P(("dp", "expert", "mp"), None),
        P(),
        P("dp", ("expert", "mp"), None),
        P("dp", ("expert", "mp"), None),
        P(("dp", "expert", "mp"), None),
        P(("dp", "expert", "mp"), None),
        P(("dp", "expert"), "mp"),
        P(("dp", "expert"), "mp"),
        P(("dp", "expert"), "mp"),
        P(),
        P(None, "mp"),
    )
    out_specs = (P(("dp", "expert", "mp"), None), P(("dp", "expert"), "mp"))
    return jax.shard_map(
        on_device, mesh=mesh, in_specs=in_specs, out_specs=out_specs, check_vma=False
    )
```

```python
import jax
import jax.numpy as jnp
from jax import lax
from jax.sharding import PartitionSpec as P


def rms_scale(values, gain):
    wide = values.astype(jnp.float32)
    mean_sq = jnp.mean(wide * wide, axis=-1, keepdims=True)
    return (wide * lax.rsqrt(mean_sq + 1e-06) * gain).astype(jnp.bfloat16)


def expert_part(rows, gate_up_w, down_w):
    quarter = down_w.shape[1]
    gate_up = jnp.dot(rows, gate_up_w, preferred_element_type=jnp.float32)
    act = (jax.nn.silu(gate_up[:, :quarter]) * gate_up[:, quarter:]).astype(jnp.bfloat16)
    return lax.dot_general(
        act, down_w, (((1,), (1,)), ((), ())), preferred_element_type=jnp.float32
    )


def on_device(
    hidden,
    norm_gain,
    expert_in,
    expert_out,
    expert_ids,
    gate_levels,
    shared_gate,
    shared_up,
    shared_down,
    next_gain,
    kv_weight,
):
    tok_rows, width = hidden.shape
    top = expert_ids.shape[1]
    n_mp = lax.axis_size("mp")
    n_groups = lax.axis_size(("dp", "expert"))
    capacity = min(tok_rows, (2 * tok_rows * top + n_groups - 1) // n_groups)
    local_e, local_rows, double = expert_in.shape
    full_ff = double // 2
    quarter = full_ff // n_mp
    in_cast = (
        expert_in.astype(jnp.bfloat16)
        .reshape(local_e, local_rows, 2, n_mp, quarter)
        .transpose(0, 3, 1, 2, 4)
    )
    out_cast = (
        expert_out.astype(jnp.bfloat16)
        .reshape(local_e, local_rows, n_mp, quarter)
        .transpose(0, 2, 1, 3)
    )
    in_send = in_cast.reshape(local_e * n_mp, local_rows, 2, quarter)
    out_send = out_cast.reshape(local_e * n_mp, local_rows, quarter)
    in_recv, out_recv = (
        lax.all_to_all(in_send, ("expert", "mp"), split_axis=0, concat_axis=1, tiled=True),
        lax.all_to_all(out_send, ("expert", "mp"), split_axis=0, concat_axis=1, tiled=True),
    )
    gate_up_w = in_recv.reshape(width, 2 * quarter)
    down_w = out_recv.reshape(width, quarter)
    normed = rms_scale(hidden, norm_gain)
    levels = gate_levels.astype(jnp.float32)
    gate_weights = levels / jnp.sum(levels, axis=1, keepdims=True)
    flat_ids = expert_ids.reshape(-1)
    pairs = flat_ids.shape[0]
    onehot = (flat_ids[:, None] == jnp.arange(n_groups, dtype=jnp.int32)[None, :]).astype(jnp.int32)
    before = jnp.cumsum(onehot, axis=0) - onehot
    slot_of_pair = jnp.sum(before * onehot, axis=1)
    target = flat_ids * capacity + slot_of_pair
    token_of_pair = jnp.arange(pairs, dtype=jnp.int32) // top
    slot_ids = jnp.arange(n_groups * capacity, dtype=jnp.int32)
    token_slot = target.reshape(tok_rows, top)[:, :, None] == slot_ids[None, None, :]
    slot_token = jnp.any(token_slot, axis=1).astype(jnp.bfloat16)
    send = lax.dot_general(
        slot_token, normed, (((0,), (0,)), ((), ())), preferred_element_type=jnp.float32
    ).astype(jnp.bfloat16)
    n_chunks = 2 if capacity % 2 == 0 else 1
    chunk = capacity // n_chunks
    send = send.reshape(n_groups, capacity, width)
    received = [
        lax.all_to_all(
            send[:, c * chunk : (c + 1) * chunk],
            ("dp", "expert"),
            split_axis=0,
            concat_axis=0,
            tiled=True,
        )
        for c in range(n_chunks)
    ]
    shared_cols = shared_gate.shape[1]
    shared_cat = jnp.concatenate([shared_gate, shared_up, shared_down], axis=1)
    shared_cat = lax.all_gather(shared_cat, "dp", axis=0, tiled=False)
    shared_cat = lax.all_gather(shared_cat, "expert", axis=1, tiled=False)
    shared_cat = shared_cat.reshape(width, 3 * shared_cols)
    group_rows = lax.all_gather(normed, "mp", axis=0, tiled=True)
    kv_cols = kv_weight.shape[1]
    kv_full = lax.all_to_all(
        jnp.broadcast_to(kv_weight[None], (n_mp,) + kv_weight.shape), "mp", 0, 0, tiled=True
    )
    received[0], shared_cat, group_rows, kv_full = lax.optimization_barrier(
        (received[0], shared_cat, group_rows, kv_full)
    )
    back = []
    for c in range(n_chunks):
        slots_here = received[c].reshape(n_groups * chunk, width)
        rows = lax.all_gather(slots_here, "mp", axis=0, tiled=True)
        summed = lax.psum_scatter(
            expert_part(rows, gate_up_w, down_w).astype(jnp.bfloat16),
            "mp",
            scatter_dimension=0,
            tiled=True,
        )
        back.append(
            lax.all_to_all(
                summed.reshape(n_groups, chunk, width),
                ("dp", "expert"),
                split_axis=0,
                concat_axis=0,
                tiled=True,
            )
        )
    back = jnp.concatenate(back, axis=1).reshape(n_groups * capacity, width)
    slot_weight = jnp.sum(jnp.where(token_slot, gate_weights[:, :, None], 0.0), axis=1)
    routed = jnp.dot(
        slot_weight,
        back.astype(jnp.float32),
        precision=lax.Precision.HIGHEST,
        preferred_element_type=jnp.float32,
    )
    gate_w = shared_cat[:, :shared_cols]
    up_w = shared_cat[:, shared_cols : 2 * shared_cols]
    down_s = shared_cat[:, 2 * shared_cols :]
    rows = group_rows
    gate_part = jnp.dot(rows, gate_w, preferred_element_type=jnp.float32)
    up_part = jnp.dot(rows, up_w, preferred_element_type=jnp.float32)
    act = (jax.nn.silu(gate_part) * up_part).astype(jnp.bfloat16)
    shared_out = lax.psum_scatter(
        lax.dot_general(act, down_s, (((1,), (1,)), ((), ())), preferred_element_type=jnp.float32),
        "mp",
        scatter_dimension=0,
        tiled=True,
    )
    layer_out = (hidden.astype(jnp.float32) + routed + shared_out).astype(jnp.bfloat16)
    next_rows = rms_scale(layer_out, next_gain)
    kv_full = kv_full.transpose(1, 0, 2).reshape(width, n_mp * kv_cols)
    kv_local = jnp.dot(next_rows, kv_full, preferred_element_type=jnp.float32).astype(
        jnp.bfloat16
    )
    kv_send = kv_local.reshape(tok_rows, n_mp, kv_cols).transpose(1, 0, 2)
    kv_latent = lax.all_to_all(kv_send, "mp", 0, 0, tiled=True).reshape(
        n_mp * tok_rows, kv_cols
    )
    return (layer_out, kv_latent)


def solution(mesh):
    in_specs = (
        P(("dp", "expert", "mp"), None),
        P(),
        P("dp", ("expert", "mp"), None),
        P("dp", ("expert", "mp"), None),
        P(("dp", "expert", "mp"), None),
        P(("dp", "expert", "mp"), None),
        P(("dp", "expert"), "mp"),
        P(("dp", "expert"), "mp"),
        P(("dp", "expert"), "mp"),
        P(),
        P(None, "mp"),
    )
    out_specs = (P(("dp", "expert", "mp"), None), P(("dp", "expert"), "mp"))
    return jax.shard_map(
        on_device, mesh=mesh, in_specs=in_specs, out_specs=out_specs, check_vma=False
    )
```

```python
import jax
import jax.numpy as jnp
from jax import lax
from jax.sharding import PartitionSpec as P


def rms_scale(values, gain):
    wide = values.astype(jnp.float32)
    mean_sq = jnp.mean(wide * wide, axis=-1, keepdims=True)
    return (wide * lax.rsqrt(mean_sq + 1e-06) * gain).astype(jnp.bfloat16)


def expert_part(rows, gate_up_w, down_w):
    quarter = down_w.shape[1]
    gate_up = jnp.dot(rows, gate_up_w, preferred_element_type=jnp.float32)
    act = (jax.nn.silu(gate_up[:, :quarter]) * gate_up[:, quarter:]).astype(jnp.bfloat16)
    return lax.dot_general(
        act, down_w, (((1,), (1,)), ((), ())), preferred_element_type=jnp.float32
    )


def on_device(
    hidden,
    norm_gain,
    expert_in,
    expert_out,
    expert_ids,
    gate_levels,
    shared_gate,
    shared_up,
    shared_down,
    next_gain,
    kv_weight,
):
    tok_rows, width = hidden.shape
    top = expert_ids.shape[1]
    n_mp = lax.axis_size("mp")
    n_groups = lax.axis_size(("dp", "expert"))
    capacity = min(tok_rows, (2 * tok_rows * top + n_groups - 1) // n_groups)
    local_e, local_rows, double = expert_in.shape
    full_ff = double // 2
    quarter = full_ff // n_mp
    in_cast = (
        expert_in.astype(jnp.bfloat16)
        .reshape(local_e, local_rows, 2, n_mp, quarter)
        .transpose(0, 3, 1, 2, 4)
    )
    out_cast = (
        expert_out.astype(jnp.bfloat16)
        .reshape(local_e, local_rows, n_mp, quarter)
        .transpose(0, 2, 1, 3)
    )
    in_send = in_cast.reshape(local_e * n_mp, local_rows, 2, quarter)
    out_send = out_cast.reshape(local_e * n_mp, local_rows, quarter)
    in_recv, out_recv = (
        lax.all_to_all(in_send, ("expert", "mp"), split_axis=0, concat_axis=1, tiled=True),
        lax.all_to_all(out_send, ("expert", "mp"), split_axis=0, concat_axis=1, tiled=True),
    )
    normed = rms_scale(hidden, norm_gain)
    levels = gate_levels.astype(jnp.float32)
    gate_weights = levels / jnp.sum(levels, axis=1, keepdims=True)
    flat_ids = expert_ids.reshape(-1)
    pairs = flat_ids.shape[0]
    onehot = (flat_ids[:, None] == jnp.arange(n_groups, dtype=jnp.int32)[None, :]).astype(jnp.int32)
    before = jnp.cumsum(onehot, axis=0) - onehot
    slot_of_pair = jnp.sum(before * onehot, axis=1)
    target = flat_ids * capacity + slot_of_pair
    token_of_pair = jnp.arange(pairs, dtype=jnp.int32) // top
    slot_ids = jnp.arange(n_groups * capacity, dtype=jnp.int32)
    token_slot = target.reshape(tok_rows, top)[:, :, None] == slot_ids[None, None, :]
    slot_token = jnp.any(token_slot, axis=1).astype(jnp.bfloat16)
    send = lax.dot_general(
        slot_token, normed, (((0,), (0,)), ((), ())), preferred_element_type=jnp.float32
    ).astype(jnp.bfloat16)
    n_chunks = 2 if capacity % 2 == 0 else 1
    chunk = capacity // n_chunks
    send = send.reshape(n_groups, capacity, width)
    received = [
        lax.all_to_all(
            send[:, c * chunk : (c + 1) * chunk],
            ("dp", "expert"),
            split_axis=0,
            concat_axis=0,
            tiled=True,
        )
        for c in range(n_chunks)
    ]
    shared_cols = shared_gate.shape[1]
    shared_cat = jnp.concatenate([shared_gate, shared_up, shared_down], axis=1)
    shared_cat = lax.all_gather(shared_cat, "dp", axis=0, tiled=False)
    shared_cat = lax.all_gather(shared_cat, "expert", axis=1, tiled=False)
    shared_cat = shared_cat.reshape(width, 3 * shared_cols)
    group_rows = lax.all_gather(normed, "mp", axis=0, tiled=True)
    kv_cols = kv_weight.shape[1]
    kv_full = lax.all_to_all(
        jnp.broadcast_to(kv_weight[None], (n_mp,) + kv_weight.shape), "mp", 0, 0, tiled=True
    )
    received[0], shared_cat, group_rows, kv_full, in_recv, out_recv = lax.optimization_barrier(
        (received[0], shared_cat, group_rows, kv_full, in_recv, out_recv)
    )
    gate_up_w = in_recv.reshape(width, 2 * quarter)
    down_w = out_recv.reshape(width, quarter)
    back = []
    for c in range(n_chunks):
        slots_here = received[c].reshape(n_groups * chunk, width)
        rows = lax.all_gather(slots_here, "mp", axis=0, tiled=True)
        summed = lax.psum_scatter(
            expert_part(rows, gate_up_w, down_w).astype(jnp.bfloat16),
            "mp",
            scatter_dimension=0,
            tiled=True,
        )
        back.append(
            lax.all_to_all(
                summed.reshape(n_groups, chunk, width),
                ("dp", "expert"),
                split_axis=0,
                concat_axis=0,
                tiled=True,
            )
        )
    back = jnp.concatenate(back, axis=1).reshape(n_groups * capacity, width)
    slot_weight = jnp.sum(jnp.where(token_slot, gate_weights[:, :, None], 0.0), axis=1)
    routed = jnp.dot(
        slot_weight,
        back.astype(jnp.float32),
        precision=lax.Precision.HIGHEST,
        preferred_element_type=jnp.float32,
    )
    gate_w = shared_cat[:, :shared_cols]
    up_w = shared_cat[:, shared_cols : 2 * shared_cols]
    down_s = shared_cat[:, 2 * shared_cols :]
    rows = group_rows
    gate_part = jnp.dot(rows, gate_w, preferred_element_type=jnp.float32)
    up_part = jnp.dot(rows, up_w, preferred_element_type=jnp.float32)
    act = (jax.nn.silu(gate_part) * up_part).astype(jnp.bfloat16)
    shared_out = lax.psum_scatter(
        lax.dot_general(act, down_s, (((1,), (1,)), ((), ())), preferred_element_type=jnp.float32),
        "mp",
        scatter_dimension=0,
        tiled=True,
    )
    layer_out = (hidden.astype(jnp.float32) + routed + shared_out).astype(jnp.bfloat16)
    next_rows = rms_scale(layer_out, next_gain)
    kv_full = kv_full.transpose(1, 0, 2).reshape(width, n_mp * kv_cols)
    kv_local = jnp.dot(next_rows, kv_full, preferred_element_type=jnp.float32).astype(
        jnp.bfloat16
    )
    kv_send = kv_local.reshape(tok_rows, n_mp, kv_cols).transpose(1, 0, 2)
    kv_latent = lax.all_to_all(kv_send, "mp", 0, 0, tiled=True).reshape(
        n_mp * tok_rows, kv_cols
    )
    return (layer_out, kv_latent)


def solution(mesh):
    in_specs = (
        P(("dp", "expert", "mp"), None),
        P(),
        P("dp", ("expert", "mp"), None),
        P("dp", ("expert", "mp"), None),
        P(("dp", "expert", "mp"), None),
        P(("dp", "expert", "mp"), None),
        P(("dp", "expert"), "mp"),
        P(("dp", "expert"), "mp"),
        P(("dp", "expert"), "mp"),
        P(),
        P(None, "mp"),
    )
    out_specs = (P(("dp", "expert", "mp"), None), P(("dp", "expert"), "mp"))
    return jax.shard_map(
        on_device, mesh=mesh, in_specs=in_specs, out_specs=out_specs, check_vma=False
    )
```

```python
import jax
import jax.numpy as jnp
from jax import lax
from jax.sharding import PartitionSpec as P


def rms_scale(values, gain):
    wide = values.astype(jnp.float32)
    mean_sq = jnp.mean(wide * wide, axis=-1, keepdims=True)
    return (wide * lax.rsqrt(mean_sq + 1e-06) * gain).astype(jnp.bfloat16)


def expert_part(rows, gate_up_w, down_w):
    quarter = down_w.shape[1]
    gate_up = jnp.dot(rows, gate_up_w, preferred_element_type=jnp.float32)
    act = (jax.nn.silu(gate_up[:, :quarter]) * gate_up[:, quarter:]).astype(jnp.bfloat16)
    return lax.dot_general(
        act, down_w, (((1,), (1,)), ((), ())), preferred_element_type=jnp.float32
    )


def on_device(
    hidden,
    norm_gain,
    expert_in,
    expert_out,
    expert_ids,
    gate_levels,
    shared_gate,
    shared_up,
    shared_down,
    next_gain,
    kv_weight,
):
    tok_rows, width = hidden.shape
    top = expert_ids.shape[1]
    n_mp = lax.axis_size("mp")
    n_groups = lax.axis_size(("dp", "expert"))
    capacity = min(tok_rows, (2 * tok_rows * top + n_groups - 1) // n_groups)
    local_e, local_rows, double = expert_in.shape
    full_ff = double // 2
    quarter = full_ff // n_mp
    in_cast = (
        expert_in.astype(jnp.bfloat16)
        .reshape(local_e, local_rows, 2, n_mp, quarter)
        .transpose(0, 3, 1, 2, 4)
    )
    out_cast = (
        expert_out.astype(jnp.bfloat16)
        .reshape(local_e, local_rows, n_mp, quarter)
        .transpose(0, 2, 1, 3)
    )
    in_send = in_cast.reshape(local_e * n_mp, local_rows, 2, quarter)
    out_send = out_cast.reshape(local_e * n_mp, local_rows, quarter)
    in_recv, out_recv = (
        lax.all_to_all(in_send, ("expert", "mp"), split_axis=0, concat_axis=1, tiled=True),
        lax.all_to_all(out_send, ("expert", "mp"), split_axis=0, concat_axis=1, tiled=True),
    )
    gate_up_w = in_recv.reshape(width, 2 * quarter)
    down_w = out_recv.reshape(width, quarter)
    normed = rms_scale(hidden, norm_gain)
    levels = gate_levels.astype(jnp.float32)
    gate_weights = levels / jnp.sum(levels, axis=1, keepdims=True)
    flat_ids = expert_ids.reshape(-1)
    pairs = flat_ids.shape[0]
    onehot = (flat_ids[:, None] == jnp.arange(n_groups, dtype=jnp.int32)[None, :]).astype(jnp.int32)
    before = jnp.cumsum(onehot, axis=0) - onehot
    slot_of_pair = jnp.sum(before * onehot, axis=1)
    target = flat_ids * capacity + slot_of_pair
    token_of_pair = jnp.arange(pairs, dtype=jnp.int32) // top
    slot_ids = jnp.arange(n_groups * capacity, dtype=jnp.int32)
    token_slot = target.reshape(tok_rows, top)[:, :, None] == slot_ids[None, None, :]
    slot_token = jnp.any(token_slot, axis=1).astype(jnp.bfloat16)
    send = lax.dot_general(
        slot_token, normed, (((0,), (0,)), ((), ())), preferred_element_type=jnp.float32
    ).astype(jnp.bfloat16)
    bounds = (0, 2 * capacity // 3, capacity) if capacity >= 3 else (0, capacity)
    spans = list(zip(bounds[:-1], bounds[1:]))
    send = send.reshape(n_groups, capacity, width)
    received = [
        lax.all_to_all(
            send[:, lo:hi],
            ("dp", "expert"),
            split_axis=0,
            concat_axis=0,
            tiled=True,
        )
        for lo, hi in spans
    ]
    shared_cols = shared_gate.shape[1]
    shared_cat = jnp.concatenate([shared_gate, shared_up, shared_down], axis=1)
    shared_cat = lax.all_gather(shared_cat, "dp", axis=0, tiled=False)
    shared_cat = lax.all_gather(shared_cat, "expert", axis=1, tiled=False)
    shared_cat = shared_cat.reshape(width, 3 * shared_cols)
    group_rows = lax.all_gather(normed, "mp", axis=0, tiled=True)
    kv_cols = kv_weight.shape[1]
    kv_full = lax.all_to_all(
        jnp.broadcast_to(kv_weight[None], (n_mp,) + kv_weight.shape), "mp", 0, 0, tiled=True
    )
    received[0], shared_cat, group_rows, kv_full = lax.optimization_barrier(
        (received[0], shared_cat, group_rows, kv_full)
    )
    back = []
    for c, (lo, hi) in enumerate(spans):
        chunk = hi - lo
        slots_here = received[c].reshape(n_groups * chunk, width)
        rows = lax.all_gather(slots_here, "mp", axis=0, tiled=True)
        summed = lax.psum_scatter(
            expert_part(rows, gate_up_w, down_w).astype(jnp.bfloat16),
            "mp",
            scatter_dimension=0,
            tiled=True,
        )
        back.append(
            lax.all_to_all(
                summed.reshape(n_groups, chunk, width),
                ("dp", "expert"),
                split_axis=0,
                concat_axis=0,
                tiled=True,
            )
        )
    back = jnp.concatenate(back, axis=1).reshape(n_groups * capacity, width)
    slot_weight = jnp.sum(jnp.where(token_slot, gate_weights[:, :, None], 0.0), axis=1)
    routed = jnp.dot(
        slot_weight,
        back.astype(jnp.float32),
        precision=lax.Precision.HIGHEST,
        preferred_element_type=jnp.float32,
    )
    gate_w = shared_cat[:, :shared_cols]
    up_w = shared_cat[:, shared_cols : 2 * shared_cols]
    down_s = shared_cat[:, 2 * shared_cols :]
    rows = group_rows
    gate_part = jnp.dot(rows, gate_w, preferred_element_type=jnp.float32)
    up_part = jnp.dot(rows, up_w, preferred_element_type=jnp.float32)
    act = (jax.nn.silu(gate_part) * up_part).astype(jnp.bfloat16)
    shared_out = lax.psum_scatter(
        lax.dot_general(act, down_s, (((1,), (1,)), ((), ())), preferred_element_type=jnp.float32),
        "mp",
        scatter_dimension=0,
        tiled=True,
    )
    layer_out = (hidden.astype(jnp.float32) + routed + shared_out).astype(jnp.bfloat16)
    next_rows = rms_scale(layer_out, next_gain)
    kv_full = kv_full.transpose(1, 0, 2).reshape(width, n_mp * kv_cols)
    kv_local = jnp.dot(next_rows, kv_full, preferred_element_type=jnp.float32).astype(
        jnp.bfloat16
    )
    kv_send = kv_local.reshape(tok_rows, n_mp, kv_cols).transpose(1, 0, 2)
    kv_latent = lax.all_to_all(kv_send, "mp", 0, 0, tiled=True).reshape(
        n_mp * tok_rows, kv_cols
    )
    return (layer_out, kv_latent)


def solution(mesh):
    in_specs = (
        P(("dp", "expert", "mp"), None),
        P(),
        P("dp", ("expert", "mp"), None),
        P("dp", ("expert", "mp"), None),
        P(("dp", "expert", "mp"), None),
        P(("dp", "expert", "mp"), None),
        P(("dp", "expert"), "mp"),
        P(("dp", "expert"), "mp"),
        P(("dp", "expert"), "mp"),
        P(),
        P(None, "mp"),
    )
    out_specs = (P(("dp", "expert", "mp"), None), P(("dp", "expert"), "mp"))
    return jax.shard_map(
        on_device, mesh=mesh, in_specs=in_specs, out_specs=out_specs, check_vma=False
    )
```

```python
import jax
import jax.numpy as jnp
from jax import lax
from jax.sharding import PartitionSpec as P


def rms_scale(values, gain):
    wide = values.astype(jnp.float32)
    mean_sq = jnp.mean(wide * wide, axis=-1, keepdims=True)
    return (wide * lax.rsqrt(mean_sq + 1e-06) * gain).astype(jnp.bfloat16)


def expert_part(rows, gate_up_w, down_w):
    quarter = down_w.shape[1]
    gate_up = jnp.dot(rows, gate_up_w, preferred_element_type=jnp.float32)
    act = (jax.nn.silu(gate_up[:, :quarter]) * gate_up[:, quarter:]).astype(jnp.bfloat16)
    return lax.dot_general(
        act, down_w, (((1,), (1,)), ((), ())), preferred_element_type=jnp.float32
    )


def on_device(
    hidden,
    norm_gain,
    expert_in,
    expert_out,
    expert_ids,
    gate_levels,
    shared_gate,
    shared_up,
    shared_down,
    next_gain,
    kv_weight,
):
    tok_rows, width = hidden.shape
    top = expert_ids.shape[1]
    n_mp = lax.axis_size("mp")
    n_groups = lax.axis_size(("dp", "expert"))
    capacity = min(tok_rows, (2 * tok_rows * top + n_groups - 1) // n_groups)
    local_e, local_rows, double = expert_in.shape
    full_ff = double // 2
    quarter = full_ff // n_mp
    in_cast = (
        expert_in.astype(jnp.bfloat16)
        .reshape(local_e, local_rows, 2, n_mp, quarter)
        .transpose(0, 3, 1, 2, 4)
    )
    out_cast = (
        expert_out.astype(jnp.bfloat16)
        .reshape(local_e, local_rows, n_mp, quarter)
        .transpose(0, 2, 1, 3)
    )
    in_send = in_cast.reshape(local_e * n_mp, local_rows, 2, quarter)
    out_send = out_cast.reshape(local_e * n_mp, local_rows, quarter)
    in_recv, out_recv = (
        lax.all_to_all(in_send, ("expert", "mp"), split_axis=0, concat_axis=1, tiled=True),
        lax.all_to_all(out_send, ("expert", "mp"), split_axis=0, concat_axis=1, tiled=True),
    )
    gate_up_w = in_recv.reshape(width, 2 * quarter)
    down_w = out_recv.reshape(width, quarter)
    normed = rms_scale(hidden, norm_gain)
    levels = gate_levels.astype(jnp.float32)
    gate_weights = levels / jnp.sum(levels, axis=1, keepdims=True)
    flat_ids = expert_ids.reshape(-1)
    pairs = flat_ids.shape[0]
    onehot = (flat_ids[:, None] == jnp.arange(n_groups, dtype=jnp.int32)[None, :]).astype(jnp.int32)
    before = jnp.cumsum(onehot, axis=0) - onehot
    slot_of_pair = jnp.sum(before * onehot, axis=1)
    target = flat_ids * capacity + slot_of_pair
    token_of_pair = jnp.arange(pairs, dtype=jnp.int32) // top
    slot_ids = jnp.arange(n_groups * capacity, dtype=jnp.int32)
    token_slot = target.reshape(tok_rows, top)[:, :, None] == slot_ids[None, None, :]
    slot_token = jnp.any(token_slot, axis=1).astype(jnp.bfloat16)
    send = lax.dot_general(
        slot_token, normed, (((0,), (0,)), ((), ())), preferred_element_type=jnp.float32
    ).astype(jnp.bfloat16)
    bounds = (0, 3 * capacity // 4, capacity) if capacity >= 4 else (0, capacity)
    spans = list(zip(bounds[:-1], bounds[1:]))
    send = send.reshape(n_groups, capacity, width)
    received = [
        lax.all_to_all(
            send[:, lo:hi],
            ("dp", "expert"),
            split_axis=0,
            concat_axis=0,
            tiled=True,
        )
        for lo, hi in spans
    ]
    shared_cols = shared_gate.shape[1]
    shared_cat = jnp.concatenate([shared_gate, shared_up, shared_down], axis=1)
    shared_cat = lax.all_gather(shared_cat, "dp", axis=0, tiled=False)
    shared_cat = lax.all_gather(shared_cat, "expert", axis=1, tiled=False)
    shared_cat = shared_cat.reshape(width, 3 * shared_cols)
    group_rows = lax.all_gather(normed, "mp", axis=0, tiled=True)
    kv_cols = kv_weight.shape[1]
    kv_full = lax.all_to_all(
        jnp.broadcast_to(kv_weight[None], (n_mp,) + kv_weight.shape), "mp", 0, 0, tiled=True
    )
    received[0], shared_cat, group_rows, kv_full = lax.optimization_barrier(
        (received[0], shared_cat, group_rows, kv_full)
    )
    back = []
    for c, (lo, hi) in enumerate(spans):
        chunk = hi - lo
        slots_here = received[c].reshape(n_groups * chunk, width)
        rows = lax.all_gather(slots_here, "mp", axis=0, tiled=True)
        summed = lax.psum_scatter(
            expert_part(rows, gate_up_w, down_w).astype(jnp.bfloat16),
            "mp",
            scatter_dimension=0,
            tiled=True,
        )
        back.append(
            lax.all_to_all(
                summed.reshape(n_groups, chunk, width),
                ("dp", "expert"),
                split_axis=0,
                concat_axis=0,
                tiled=True,
            )
        )
    back = jnp.concatenate(back, axis=1).reshape(n_groups * capacity, width)
    slot_weight = jnp.sum(jnp.where(token_slot, gate_weights[:, :, None], 0.0), axis=1)
    routed = jnp.dot(
        slot_weight,
        back.astype(jnp.float32),
        precision=lax.Precision.HIGHEST,
        preferred_element_type=jnp.float32,
    )
    gate_w = shared_cat[:, :shared_cols]
    up_w = shared_cat[:, shared_cols : 2 * shared_cols]
    down_s = shared_cat[:, 2 * shared_cols :]
    rows = group_rows
    gate_part = jnp.dot(rows, gate_w, preferred_element_type=jnp.float32)
    up_part = jnp.dot(rows, up_w, preferred_element_type=jnp.float32)
    act = (jax.nn.silu(gate_part) * up_part).astype(jnp.bfloat16)
    shared_out = lax.psum_scatter(
        lax.dot_general(act, down_s, (((1,), (1,)), ((), ())), preferred_element_type=jnp.float32),
        "mp",
        scatter_dimension=0,
        tiled=True,
    )
    layer_out = (hidden.astype(jnp.float32) + routed + shared_out).astype(jnp.bfloat16)
    next_rows = rms_scale(layer_out, next_gain)
    kv_full = kv_full.transpose(1, 0, 2).reshape(width, n_mp * kv_cols)
    kv_local = jnp.dot(next_rows, kv_full, preferred_element_type=jnp.float32).astype(
        jnp.bfloat16
    )
    kv_send = kv_local.reshape(tok_rows, n_mp, kv_cols).transpose(1, 0, 2)
    kv_latent = lax.all_to_all(kv_send, "mp", 0, 0, tiled=True).reshape(
        n_mp * tok_rows, kv_cols
    )
    return (layer_out, kv_latent)


def solution(mesh):
    in_specs = (
        P(("dp", "expert", "mp"), None),
        P(),
        P("dp", ("expert", "mp"), None),
        P("dp", ("expert", "mp"), None),
        P(("dp", "expert", "mp"), None),
        P(("dp", "expert", "mp"), None),
        P(("dp", "expert"), "mp"),
        P(("dp", "expert"), "mp"),
        P(("dp", "expert"), "mp"),
        P(),
        P(None, "mp"),
    )
    out_specs = (P(("dp", "expert", "mp"), None), P(("dp", "expert"), "mp"))
    return jax.shard_map(
        on_device, mesh=mesh, in_specs=in_specs, out_specs=out_specs, check_vma=False
    )
```

```python
import jax
import jax.numpy as jnp
from jax import lax
from jax.sharding import PartitionSpec as P


def rms_scale(values, gain):
    wide = values.astype(jnp.float32)
    mean_sq = jnp.mean(wide * wide, axis=-1, keepdims=True)
    return (wide * lax.rsqrt(mean_sq + 1e-06) * gain).astype(jnp.bfloat16)


def expert_part(rows, gate_up_w, down_w):
    quarter = down_w.shape[1]
    gate_up = jnp.dot(rows, gate_up_w, preferred_element_type=jnp.float32)
    act = (jax.nn.silu(gate_up[:, :quarter]) * gate_up[:, quarter:]).astype(jnp.bfloat16)
    return lax.dot_general(
        act, down_w, (((1,), (1,)), ((), ())), preferred_element_type=jnp.float32
    )


def on_device(
    hidden,
    norm_gain,
    expert_in,
    expert_out,
    expert_ids,
    gate_levels,
    shared_gate,
    shared_up,
    shared_down,
    next_gain,
    kv_weight,
):
    tok_rows, width = hidden.shape
    top = expert_ids.shape[1]
    n_mp = lax.axis_size("mp")
    n_groups = lax.axis_size(("dp", "expert"))
    capacity = min(tok_rows, (2 * tok_rows * top + n_groups - 1) // n_groups)
    local_e, local_rows, double = expert_in.shape
    full_ff = double // 2
    quarter = full_ff // n_mp
    in_cast = (
        expert_in.astype(jnp.bfloat16)
        .reshape(local_e, local_rows, 2, n_mp, quarter)
        .transpose(0, 3, 1, 2, 4)
    )
    out_cast = (
        expert_out.astype(jnp.bfloat16)
        .reshape(local_e, local_rows, n_mp, quarter)
        .transpose(0, 2, 1, 3)
    )
    in_send = in_cast.reshape(local_e * n_mp, local_rows, 2, quarter)
    out_send = out_cast.reshape(local_e * n_mp, local_rows, quarter)
    in_recv, out_recv = (
        lax.all_to_all(in_send, ("expert", "mp"), split_axis=0, concat_axis=1, tiled=True),
        lax.all_to_all(out_send, ("expert", "mp"), split_axis=0, concat_axis=1, tiled=True),
    )
    gate_up_w = in_recv.reshape(width, 2 * quarter)
    down_w = out_recv.reshape(width, quarter)
    normed = rms_scale(hidden, norm_gain)
    levels = gate_levels.astype(jnp.float32)
    gate_weights = levels / jnp.sum(levels, axis=1, keepdims=True)
    flat_ids = expert_ids.reshape(-1)
    pairs = flat_ids.shape[0]
    onehot = (flat_ids[:, None] == jnp.arange(n_groups, dtype=jnp.int32)[None, :]).astype(jnp.int32)
    before = jnp.cumsum(onehot, axis=0) - onehot
    slot_of_pair = jnp.sum(before * onehot, axis=1)
    target = flat_ids * capacity + slot_of_pair
    token_of_pair = jnp.arange(pairs, dtype=jnp.int32) // top
    slot_ids = jnp.arange(n_groups * capacity, dtype=jnp.int32)
    token_slot = target.reshape(tok_rows, top)[:, :, None] == slot_ids[None, None, :]
    slot_token = jnp.any(token_slot, axis=1).astype(jnp.bfloat16)
    send = lax.dot_general(
        slot_token, normed, (((0,), (0,)), ((), ())), preferred_element_type=jnp.float32
    ).astype(jnp.bfloat16)
    bounds = (0, 5 * capacity // 12, capacity) if capacity >= 3 else (0, capacity)
    spans = list(zip(bounds[:-1], bounds[1:]))
    send = send.reshape(n_groups, capacity, width)
    received = [
        lax.all_to_all(
            send[:, lo:hi],
            ("dp", "expert"),
            split_axis=0,
            concat_axis=0,
            tiled=True,
        )
        for lo, hi in spans
    ]
    shared_cols = shared_gate.shape[1]
    shared_cat = jnp.concatenate([shared_gate, shared_up, shared_down], axis=1)
    shared_cat = lax.all_gather(shared_cat, "dp", axis=0, tiled=False)
    shared_cat = lax.all_gather(shared_cat, "expert", axis=1, tiled=False)
    shared_cat = shared_cat.reshape(width, 3 * shared_cols)
    group_rows = lax.all_gather(normed, "mp", axis=0, tiled=True)
    kv_cols = kv_weight.shape[1]
    kv_full = lax.all_to_all(
        jnp.broadcast_to(kv_weight[None], (n_mp,) + kv_weight.shape), "mp", 0, 0, tiled=True
    )
    received[0], shared_cat, group_rows, kv_full = lax.optimization_barrier(
        (received[0], shared_cat, group_rows, kv_full)
    )
    back = []
    for c, (lo, hi) in enumerate(spans):
        chunk = hi - lo
        slots_here = received[c].reshape(n_groups * chunk, width)
        rows = lax.all_gather(slots_here, "mp", axis=0, tiled=True)
        summed = lax.psum_scatter(
            expert_part(rows, gate_up_w, down_w).astype(jnp.bfloat16),
            "mp",
            scatter_dimension=0,
            tiled=True,
        )
        back.append(
            lax.all_to_all(
                summed.reshape(n_groups, chunk, width),
                ("dp", "expert"),
                split_axis=0,
                concat_axis=0,
                tiled=True,
            )
        )
    back = jnp.concatenate(back, axis=1).reshape(n_groups * capacity, width)
    slot_weight = jnp.sum(jnp.where(token_slot, gate_weights[:, :, None], 0.0), axis=1)
    routed = jnp.dot(
        slot_weight,
        back.astype(jnp.float32),
        precision=lax.Precision.HIGHEST,
        preferred_element_type=jnp.float32,
    )
    gate_w = shared_cat[:, :shared_cols]
    up_w = shared_cat[:, shared_cols : 2 * shared_cols]
    down_s = shared_cat[:, 2 * shared_cols :]
    rows = group_rows
    gate_part = jnp.dot(rows, gate_w, preferred_element_type=jnp.float32)
    up_part = jnp.dot(rows, up_w, preferred_element_type=jnp.float32)
    act = (jax.nn.silu(gate_part) * up_part).astype(jnp.bfloat16)
    shared_out = lax.psum_scatter(
        lax.dot_general(act, down_s, (((1,), (1,)), ((), ())), preferred_element_type=jnp.float32),
        "mp",
        scatter_dimension=0,
        tiled=True,
    )
    layer_out = (hidden.astype(jnp.float32) + routed + shared_out).astype(jnp.bfloat16)
    next_rows = rms_scale(layer_out, next_gain)
    kv_full = kv_full.transpose(1, 0, 2).reshape(width, n_mp * kv_cols)
    kv_local = jnp.dot(next_rows, kv_full, preferred_element_type=jnp.float32).astype(
        jnp.bfloat16
    )
    kv_send = kv_local.reshape(tok_rows, n_mp, kv_cols).transpose(1, 0, 2)
    kv_latent = lax.all_to_all(kv_send, "mp", 0, 0, tiled=True).reshape(
        n_mp * tok_rows, kv_cols
    )
    return (layer_out, kv_latent)


def solution(mesh):
    in_specs = (
        P(("dp", "expert", "mp"), None),
        P(),
        P("dp", ("expert", "mp"), None),
        P("dp", ("expert", "mp"), None),
        P(("dp", "expert", "mp"), None),
        P(("dp", "expert", "mp"), None),
        P(("dp", "expert"), "mp"),
        P(("dp", "expert"), "mp"),
        P(("dp", "expert"), "mp"),
        P(),
        P(None, "mp"),
    )
    out_specs = (P(("dp", "expert", "mp"), None), P(("dp", "expert"), "mp"))
    return jax.shard_map(
        on_device, mesh=mesh, in_specs=in_specs, out_specs=out_specs, check_vma=False
    )
```

```python
import jax
import jax.numpy as jnp
from jax import lax
from jax.sharding import PartitionSpec as P


def rms_scale(values, gain):
    wide = values.astype(jnp.float32)
    mean_sq = jnp.mean(wide * wide, axis=-1, keepdims=True)
    return (wide * lax.rsqrt(mean_sq + 1e-06) * gain).astype(jnp.bfloat16)


def expert_part(rows, gate_up_w, down_w):
    quarter = down_w.shape[1]
    gate_up = jnp.dot(rows, gate_up_w, preferred_element_type=jnp.float32)
    act = (jax.nn.silu(gate_up[:, :quarter]) * gate_up[:, quarter:]).astype(jnp.bfloat16)
    return lax.dot_general(
        act, down_w, (((1,), (1,)), ((), ())), preferred_element_type=jnp.float32
    )


def on_device(
    hidden,
    norm_gain,
    expert_in,
    expert_out,
    expert_ids,
    gate_levels,
    shared_gate,
    shared_up,
    shared_down,
    next_gain,
    kv_weight,
):
    tok_rows, width = hidden.shape
    top = expert_ids.shape[1]
    n_mp = lax.axis_size("mp")
    n_groups = lax.axis_size(("dp", "expert"))
    capacity = min(tok_rows, (2 * tok_rows * top + n_groups - 1) // n_groups)
    local_e, local_rows, double = expert_in.shape
    full_ff = double // 2
    quarter = full_ff // n_mp
    in_cast = (
        expert_in.astype(jnp.bfloat16)
        .reshape(local_e, local_rows, 2, n_mp, quarter)
        .transpose(0, 3, 1, 2, 4)
    )
    out_cast = (
        expert_out.astype(jnp.bfloat16)
        .reshape(local_e, local_rows, n_mp, quarter)
        .transpose(0, 2, 1, 3)
    )
    in_send = in_cast.reshape(local_e * n_mp, local_rows, 2, quarter)
    out_send = out_cast.reshape(local_e * n_mp, local_rows, quarter)
    in_recv, out_recv = (
        lax.all_to_all(in_send, ("expert", "mp"), split_axis=0, concat_axis=1, tiled=True),
        lax.all_to_all(out_send, ("expert", "mp"), split_axis=0, concat_axis=1, tiled=True),
    )
    gate_up_w = in_recv.reshape(width, 2 * quarter)
    down_w = out_recv.reshape(width, quarter)
    normed = rms_scale(hidden, norm_gain)
    levels = gate_levels.astype(jnp.float32)
    gate_weights = levels / jnp.sum(levels, axis=1, keepdims=True)
    flat_ids = expert_ids.reshape(-1)
    pairs = flat_ids.shape[0]
    onehot = (flat_ids[:, None] == jnp.arange(n_groups, dtype=jnp.int32)[None, :]).astype(jnp.int32)
    before = jnp.cumsum(onehot, axis=0) - onehot
    slot_of_pair = jnp.sum(before * onehot, axis=1)
    target = flat_ids * capacity + slot_of_pair
    token_of_pair = jnp.arange(pairs, dtype=jnp.int32) // top
    slot_ids = jnp.arange(n_groups * capacity, dtype=jnp.int32)
    token_slot = target.reshape(tok_rows, top)[:, :, None] == slot_ids[None, None, :]
    slot_token = jnp.any(token_slot, axis=1).astype(jnp.bfloat16)
    send = lax.dot_general(
        slot_token, normed, (((0,), (0,)), ((), ())), preferred_element_type=jnp.float32
    ).astype(jnp.bfloat16)
    bounds = (0, 7 * capacity // 12, capacity) if capacity >= 3 else (0, capacity)
    spans = list(zip(bounds[:-1], bounds[1:]))
    send = send.reshape(n_groups, capacity, width)
    received = [
        lax.all_to_all(
            send[:, lo:hi],
            ("dp", "expert"),
            split_axis=0,
            concat_axis=0,
            tiled=True,
        )
        for lo, hi in spans
    ]
    shared_cols = shared_gate.shape[1]
    shared_cat = jnp.concatenate([shared_gate, shared_up, shared_down], axis=1)
    shared_cat = lax.all_gather(shared_cat, "dp", axis=0, tiled=False)
    shared_cat = lax.all_gather(shared_cat, "expert", axis=1, tiled=False)
    shared_cat = shared_cat.reshape(width, 3 * shared_cols)
    group_rows = lax.all_gather(normed, "mp", axis=0, tiled=True)
    kv_cols = kv_weight.shape[1]
    kv_full = lax.all_to_all(
        jnp.broadcast_to(kv_weight[None], (n_mp,) + kv_weight.shape), "mp", 0, 0, tiled=True
    )
    received[0], shared_cat, group_rows, kv_full = lax.optimization_barrier(
        (received[0], shared_cat, group_rows, kv_full)
    )
    back = []
    for c, (lo, hi) in enumerate(spans):
        chunk = hi - lo
        slots_here = received[c].reshape(n_groups * chunk, width)
        rows = lax.all_gather(slots_here, "mp", axis=0, tiled=True)
        summed = lax.psum_scatter(
            expert_part(rows, gate_up_w, down_w).astype(jnp.bfloat16),
            "mp",
            scatter_dimension=0,
            tiled=True,
        )
        back.append(
            lax.all_to_all(
                summed.reshape(n_groups, chunk, width),
                ("dp", "expert"),
                split_axis=0,
                concat_axis=0,
                tiled=True,
            )
        )
    back = jnp.concatenate(back, axis=1).reshape(n_groups * capacity, width)
    slot_weight = jnp.sum(jnp.where(token_slot, gate_weights[:, :, None], 0.0), axis=1)
    routed = jnp.dot(
        slot_weight,
        back.astype(jnp.float32),
        precision=lax.Precision.HIGHEST,
        preferred_element_type=jnp.float32,
    )
    gate_w = shared_cat[:, :shared_cols]
    up_w = shared_cat[:, shared_cols : 2 * shared_cols]
    down_s = shared_cat[:, 2 * shared_cols :]
    rows = group_rows
    gate_part = jnp.dot(rows, gate_w, preferred_element_type=jnp.float32)
    up_part = jnp.dot(rows, up_w, preferred_element_type=jnp.float32)
    act = (jax.nn.silu(gate_part) * up_part).astype(jnp.bfloat16)
    shared_out = lax.psum_scatter(
        lax.dot_general(act, down_s, (((1,), (1,)), ((), ())), preferred_element_type=jnp.float32),
        "mp",
        scatter_dimension=0,
        tiled=True,
    )
    layer_out = (hidden.astype(jnp.float32) + routed + shared_out).astype(jnp.bfloat16)
    next_rows = rms_scale(layer_out, next_gain)
    kv_full = kv_full.transpose(1, 0, 2).reshape(width, n_mp * kv_cols)
    kv_local = jnp.dot(next_rows, kv_full, preferred_element_type=jnp.float32).astype(
        jnp.bfloat16
    )
    kv_send = kv_local.reshape(tok_rows, n_mp, kv_cols).transpose(1, 0, 2)
    kv_latent = lax.all_to_all(kv_send, "mp", 0, 0, tiled=True).reshape(
        n_mp * tok_rows, kv_cols
    )
    return (layer_out, kv_latent)


def solution(mesh):
    in_specs = (
        P(("dp", "expert", "mp"), None),
        P(),
        P("dp", ("expert", "mp"), None),
        P("dp", ("expert", "mp"), None),
        P(("dp", "expert", "mp"), None),
        P(("dp", "expert", "mp"), None),
        P(("dp", "expert"), "mp"),
        P(("dp", "expert"), "mp"),
        P(("dp", "expert"), "mp"),
        P(),
        P(None, "mp"),
    )
    out_specs = (P(("dp", "expert", "mp"), None), P(("dp", "expert"), "mp"))
    return jax.shard_map(
        on_device, mesh=mesh, in_specs=in_specs, out_specs=out_specs, check_vma=False
    )
```
